32 devices in a mesh: freq: 4 (over x, core), tm: 8 (over z, y).
Axes of the slice: x: 2, y: 2, z: 4, core: 2. Of those that a mesh axis runs over, the one named last changes fastest.
Arguments:
- signal: float32 [8388608], P('tm'), may hold values from -60 to 60, as said below
- w_init: float32 [2048, 256], P('freq'), may hold values from 0.02 to 0.2
- h_init: float32 [256, 8192], P(None, 'tm'), may hold values from 0.02 to 0.2
Outputs:
- factor_w: float32 [2048, 256], P('freq')
- factor_h: float32 [256, 8192], P(None, 'tm')
The draws below stay inside these ranges and needn't reach their ends.
Inputs may be any that keep to these rules, and one draw needn't show every extreme that they name: `signal`: a broadband record with a few tones.
All inputs are finite; a program needn't handle non-finite values.
Results may differ from the reference program's by a relative error of at most 0.0004.
Values sent between devices are 32-bit elements; how exact they have to be, the bound alone decides.
No kernel may reach another device: no remote copies, remote signals or barrier semaphores. Data moves between devices by JAX's collectives and lax.ppermute only.
A program may use at most 128 MiB of HBM per device.

```python
import math
import jax
import jax.numpy as jnp
from jax import lax

WIN = 4096
HOP = 1024
K = 2048
R = 256
ITERS = 2
FRAMES = 8192


def draw_signal(key, part):
    total = FRAMES * HOP
    times = jnp.arange(total, dtype=jnp.int32)
    noise_key = jax.random.fold_in(key, 11)
    bin_key = jax.random.fold_in(key, 12)
    amp_key = jax.random.fold_in(key, 13)
    noise = jax.random.truncated_normal(noise_key, -5.0, 5.0, (total,), jnp.float32)
    amplitudes = jax.random.uniform(amp_key, (8,), jnp.float32, 0.03, 0.12)
    tone_bins = jax.random.randint(bin_key, (8,), 1, K)
    within = times % WIN
    tones = jnp.zeros((total,), jnp.float32)
    for index in range(8):
        phase = tone_bins[index] * within % WIN
        tones = tones + amplitudes[index] * jnp.sin(phase.astype(jnp.float32) * (2.0 * math.pi / WIN))
    envelope = jnp.exp(0.5 * math.log(3.0) * times.astype(jnp.float32) / total)
    return envelope * (noise + tones)


def block_scale(stream_key, extent, cuts, smallest, largest):
    loudness = 1.0
    for position, blocks in cuts:
        steps = jax.random.uniform(jax.random.fold_in(jax.random.fold_in(stream_key, 6), position), (blocks,), jnp.float32, smallest / len(cuts), largest / len(cuts))
        loudness = loudness * jnp.repeat(jnp.exp(steps), extent[position] // blocks).reshape((-1,) + (1,) * (len(extent) - 1 - position))
    return loudness


def setup_inputs(seed: int = 0) -> dict:
    keys = jax.random.split(jax.random.key(seed), 4)
    signal = draw_signal(jax.random.fold_in(keys[3], 71), 0)
    w_init = jnp.clip(jnp.exp(math.log(0.2) - 2.3025851 * jax.random.uniform(keys[1], (K, R), jnp.float32) ** block_scale(keys[1], (K, R), ((0, 4),), -0.2, 0.2)), 0.02, 0.2)
    h_init = jnp.clip(jnp.exp(math.log(0.2) - 2.3025851 * jax.random.uniform(keys[2], (R, FRAMES), jnp.float32) ** block_scale(keys[2], (R, FRAMES), ((1, 8),), -0.2, 0.2)), 0.02, 0.2)
    return {"signal": signal, "w_init": w_init, "h_init": h_init}


def dft_table(first, count):
    samples = jnp.arange(WIN, dtype=jnp.int32)
    bins = first + jnp.arange(count, dtype=jnp.int32)
    phase = (samples[:, None] * bins[None, :]) % WIN
    angle = phase.astype(jnp.float32) * (2.0 * math.pi / WIN)
    return jnp.concatenate([jnp.cos(angle), jnp.sin(angle)], axis=1).astype(jnp.bfloat16)


def hann_window():
    samples = jnp.arange(WIN, dtype=jnp.int32).astype(jnp.float32)
    return 0.5 - 0.5 * jnp.cos(samples * (2.0 * math.pi / WIN))


def reference(signal, w_init, h_init):
    steps_per = WIN // HOP
    padded = jnp.concatenate([signal, jnp.zeros(((steps_per - 1) * HOP,), jnp.float32)])
    blocks = padded.reshape(-1, HOP)
    frames = jnp.concatenate([blocks[j:j + FRAMES] for j in range(steps_per)], axis=1)
    windowed = (frames * hann_window()[None, :]).astype(jnp.bfloat16)
    table = dft_table(0, K)
    spectra = jnp.dot(windowed.astype(jnp.float32), table.astype(jnp.float32), precision=lax.Precision.HIGHEST, preferred_element_type=jnp.float32)
    real_part = spectra[:, :K]
    imag_part = spectra[:, K:]
    power = ((real_part * real_part + imag_part * imag_part) / (0.375 * WIN)).T
    factor_w = w_init
    factor_h = h_init
    for step in range(ITERS):
        model = jnp.dot(factor_w, factor_h, precision=lax.Precision.HIGHEST, preferred_element_type=jnp.float32)
        ratio = power / model
        numer = jnp.einsum("kr,kf->rf", factor_w, ratio, precision=lax.Precision.HIGHEST)
        column_sums = jnp.sum(factor_w, axis=0)
        factor_h = factor_h * numer / column_sums[:, None]
        model = jnp.dot(factor_w, factor_h, precision=lax.Precision.HIGHEST, preferred_element_type=jnp.float32)
        ratio = power / model
        spectral = jnp.einsum("kf,rf->kr", ratio, factor_h, precision=lax.Precision.HIGHEST)
        row_sums = jnp.sum(factor_h, axis=1)
        factor_w = factor_w * spectral / row_sums[None, :]
    return factor_w, factor_h
```

```python
import math

import jax
import jax.numpy as jnp
from jax import lax
from jax.sharding import PartitionSpec as P

WIN = 4096
HOP = 1024
K = 2048
ITERS = 2
HI = lax.Precision.HIGHEST


def shifted(value, axis, by):
    size = lax.axis_size(axis)
    pairs = [(i, i + by) for i in range(size) if 0 <= i + by < size]
    return lax.ppermute(value, axis, pairs)


def dft_table(first, count):
    samples = jnp.arange(WIN, dtype=jnp.int32)
    bins = first + jnp.arange(count, dtype=jnp.int32)
    phase = samples[:, None] * bins[None, :] % WIN
    angle = phase.astype(jnp.float32) * (2.0 * math.pi / WIN)
    return jnp.concatenate([jnp.cos(angle), jnp.sin(angle)], axis=1).astype(jnp.bfloat16)


def hann_window():
    samples = jnp.arange(WIN, dtype=jnp.int32).astype(jnp.float32)
    return 0.5 - 0.5 * jnp.cos(samples * (2.0 * math.pi / WIN))


def cut_frames(blocks, count):
    steps_per = WIN // HOP
    frames = jnp.concatenate([blocks[j : j + count] for j in range(steps_per)], axis=1)
    return (frames * hann_window()[None, :]).astype(jnp.bfloat16)


def spectrum(windowed, table, count):
    both = jnp.einsum("wc,fw->cf", table, windowed, preferred_element_type=jnp.float32)
    real_part = both[:count]
    imag_part = both[count:]
    return (real_part * real_part + imag_part * imag_part) / (0.375 * WIN)


def halves(x, dim, bit):
    lo, hi = jnp.split(x, 2, axis=dim)
    keep = jnp.where(bit == 0, lo, hi)
    send = jnp.where(bit == 0, hi, lo)
    return keep, send


def reduce_scatter(x, extra, axis, dim):
    n = lax.axis_size(axis)
    idx = lax.axis_index(axis)
    d = 1
    while d < n:
        bit = (idx // d) % 2
        keep, send = halves(x, dim, bit)
        pairs = [(i, i ^ d) for i in range(n)]
        got, got_extra = lax.ppermute((send, extra), axis, pairs)
        x = keep + got
        extra = extra + got_extra
        d *= 2
    return x, extra


def chunk_of(x, axis, dim):
    n = lax.axis_size(axis)
    idx = lax.axis_index(axis)
    d = 1
    while d < n:
        bit = (idx // d) % 2
        x, _ = halves(x, dim, bit)
        d *= 2
    return x


def all_gather(x, axis, dim):
    n = lax.axis_size(axis)
    idx = lax.axis_index(axis)
    d = n // 2
    while d >= 1:
        bit = (idx // d) % 2
        pairs = [(i, i ^ d) for i in range(n)]
        got = lax.ppermute(x, axis, pairs)
        first = jnp.where(bit == 0, x, got)
        second = jnp.where(bit == 0, got, x)
        x = jnp.concatenate([first, second], axis=dim)
        d //= 2
    return x


def local(signal, w_init, h_init):
    steps_per = WIN // HOP
    frames_dev = signal.shape[0] // HOP
    tail = shifted(signal[: (steps_per - 1) * HOP], "tm", -1)
    blocks = jnp.concatenate([signal, tail]).reshape(frames_dev + steps_per - 1, HOP)
    local_bins = K // lax.axis_size("freq")
    windowed = cut_frames(blocks, frames_dev)
    power = spectrum(
        windowed, dft_table(lax.axis_index("freq") * local_bins, local_bins), local_bins
    )
    factor_w = w_init
    factor_h = h_init
    for step in range(ITERS):
        model = jnp.dot(factor_w, factor_h, precision=HI, preferred_element_type=jnp.float32)
        ratio = power / model
        numer = jnp.einsum("kr,kf->rf", factor_w, ratio, precision=HI)
        column_sums = jnp.sum(factor_w, axis=0)
        numer, column_sums = reduce_scatter(numer, column_sums, "freq", 1)
        h_part = chunk_of(factor_h, "freq", 1)
        h_part = h_part * numer / column_sums[:, None]
        factor_h = all_gather(h_part, "freq", 1)
        model = jnp.dot(factor_w, factor_h, precision=HI, preferred_element_type=jnp.float32)
        ratio = power / model
        row_sums = jnp.sum(factor_h, axis=1)
        spectral = jnp.einsum("kf,rf->kr", ratio, factor_h, precision=HI)
        spectral, row_sums = reduce_scatter(spectral, row_sums, "tm", 0)
        w_part = chunk_of(factor_w, "tm", 0)
        w_part = w_part * spectral / row_sums[None, :]
        factor_w = all_gather(w_part, "tm", 0)
    return (factor_w, factor_h)


def solution(mesh):
    in_specs = (P("tm"), P("freq", None), P(None, "tm"))
    out_specs = (P("freq", None), P(None, "tm"))
    return jax.shard_map(local, mesh=mesh, in_specs=in_specs, out_specs=out_specs, check_vma=False)
```

```python
import math

import functools

import jax
import jax.numpy as jnp
from jax import lax
from jax.experimental import pallas as pl
from jax.experimental.pallas import tpu as pltpu
from jax.sharding import PartitionSpec as P

WIN = 4096
HOP = 1024
K = 2048
ITERS = 2
HI = lax.Precision.HIGHEST


def shifted(value, axis, by):
    size = lax.axis_size(axis)
    pairs = [(i, i + by) for i in range(size) if 0 <= i + by < size]
    return lax.ppermute(value, axis, pairs)


def hann_window():
    samples = jnp.arange(WIN, dtype=jnp.int32).astype(jnp.float32)
    return 0.5 - 0.5 * jnp.cos(samples * (2.0 * math.pi / WIN))


SUB = 128


def small_tables(first, count):
    bins = first + jnp.arange(count, dtype=jnp.int32)
    a = jnp.arange(WIN // SUB, dtype=jnp.int32)
    b = jnp.arange(SUB, dtype=jnp.int32)
    pa = (a[:, None] * SUB * bins[None, :]) % WIN
    pb = (b[:, None] * bins[None, :]) % WIN
    sc = 2.0 * math.pi / WIN
    ta = pa.astype(jnp.float32) * sc
    tb = pb.astype(jnp.float32) * sc
    return jnp.cos(ta), jnp.sin(ta), jnp.cos(tb), jnp.sin(tb)


def dft_kernel(sig_hbm, tail_ref, win_ref, ca_ref, sa_ref, cb_ref, sb_ref, out_ref,
               blocks, tab, acc_ref, sem, *, tf, count, frames):
    i = pl.program_id(0)

    @pl.when(i == 0)
    def _():
        copy = pltpu.make_async_copy(sig_hbm, blocks.at[pl.ds(0, frames), :], sem)
        copy.start()
        blocks[pl.ds(frames, 8), :] = tail_ref[...]
        cb = cb_ref[...]
        sb = sb_ref[...]
        for a in range(WIN // SUB):
            ca = ca_ref[a:a + 1, :]
            sa = sa_ref[a:a + 1, :]
            tab[pl.ds(a * SUB, SUB), pl.ds(0, count)] = (ca * cb - sa * sb).astype(jnp.bfloat16)
            tab[pl.ds(a * SUB, SUB), pl.ds(count, count)] = (sa * cb + ca * sb).astype(jnp.bfloat16)
        copy.wait()

    base = pl.multiple_of(i * tf, tf)
    rows = blocks[pl.ds(base, tf + 8), :]
    for j in range(WIN // HOP):
        x = (rows[j:j + tf, :] * win_ref[j:j + 1, :]).astype(jnp.bfloat16)
        part = jnp.dot(x, tab[pl.ds(j * HOP, HOP), :], preferred_element_type=jnp.float32)
        if j == 0:
            acc_ref[...] = part
        else:
            acc_ref[...] += part
    re = acc_ref[:, :count]
    im = acc_ref[:, count:]
    out_ref[...] = ((re * re + im * im) / (0.375 * WIN)).T


def power_kernel(sig2d, tail8, win4, tables, count, tf=512, interpret=False):
    frames = sig2d.shape[0]
    ca, sa, cb, sb = tables
    full = lambda shape: pl.BlockSpec(shape, lambda i: (0, 0), pipeline_mode=pl.Buffered(1))
    return pl.pallas_call(
        functools.partial(dft_kernel, tf=tf, count=count, frames=frames),
        grid=(frames // tf,),
        in_specs=[pl.BlockSpec(memory_space=pl.ANY),
                  full(tail8.shape), full(win4.shape), full(ca.shape), full(sa.shape),
                  full(cb.shape), full(sb.shape)],
        out_specs=pl.BlockSpec((count, tf), lambda i: (0, i)),
        out_shape=jax.ShapeDtypeStruct((count, frames), jnp.float32),
        scratch_shapes=[pltpu.VMEM((frames + 8, HOP), jnp.float32),
                        pltpu.VMEM((WIN, 2 * count), jnp.bfloat16),
                        pltpu.VMEM((tf, 2 * count), jnp.float32),
                        pltpu.SemaphoreType.DMA],
        compiler_params=pltpu.CompilerParams(vmem_limit_bytes=48 * 1024 * 1024,
                                             dimension_semantics=("arbitrary",)),
        interpret=interpret,
    )(sig2d, tail8, win4, ca, sa, cb, sb)


def halves(x, dim, bit):
    lo, hi = jnp.split(x, 2, axis=dim)
    keep = jnp.where(bit == 0, lo, hi)
    send = jnp.where(bit == 0, hi, lo)
    return keep, send


def reduce_scatter(x, extra, axis, dim):
    n = lax.axis_size(axis)
    idx = lax.axis_index(axis)
    d = 1
    while d < n:
        bit = (idx // d) % 2
        keep, send = halves(x, dim, bit)
        pairs = [(i, i ^ d) for i in range(n)]
        got, got_extra = lax.ppermute((send, extra), axis, pairs)
        x = keep + got
        extra = extra + got_extra
        d *= 2
    return x, extra


def chunk_of(x, axis, dim):
    n = lax.axis_size(axis)
    idx = lax.axis_index(axis)
    d = 1
    while d < n:
        bit = (idx // d) % 2
        x, _ = halves(x, dim, bit)
        d *= 2
    return x


def all_gather(x, axis, dim):
    n = lax.axis_size(axis)
    idx = lax.axis_index(axis)
    d = n // 2
    while d >= 1:
        bit = (idx // d) % 2
        pairs = [(i, i ^ d) for i in range(n)]
        got = lax.ppermute(x, axis, pairs)
        first = jnp.where(bit == 0, x, got)
        second = jnp.where(bit == 0, got, x)
        x = jnp.concatenate([first, second], axis=dim)
        d //= 2
    return x


def local(signal, w_init, h_init):
    steps_per = WIN // HOP
    frames_dev = signal.shape[0] // HOP
    tail = shifted(signal[: (steps_per - 1) * HOP], "tm", -1)
    tail8 = jnp.concatenate([tail, jnp.zeros(((8 - steps_per + 1) * HOP,), jnp.float32)])
    local_bins = K // lax.axis_size("freq")
    win4 = hann_window().reshape(steps_per, HOP)
    tables = small_tables(lax.axis_index("freq") * local_bins, local_bins)
    power = power_kernel(signal.reshape(frames_dev, HOP), tail8.reshape(8, HOP), win4, tables, local_bins)
    factor_w = w_init
    factor_h = h_init
    for step in range(ITERS):
        model = jnp.dot(factor_w, factor_h, precision=HI, preferred_element_type=jnp.float32)
        ratio = power / model
        numer = jnp.einsum("kr,kf->rf", factor_w, ratio, precision=HI)
        column_sums = jnp.sum(factor_w, axis=0)
        numer, column_sums = reduce_scatter(numer, column_sums, "freq", 1)
        h_part = chunk_of(factor_h, "freq", 1)
        h_part = h_part * numer / column_sums[:, None]
        factor_h = all_gather(h_part, "freq", 1)
        model = jnp.dot(factor_w, factor_h, precision=HI, preferred_element_type=jnp.float32)
        ratio = power / model
        row_sums = jnp.sum(factor_h, axis=1)
        spectral = jnp.einsum("kf,rf->kr", ratio, factor_h, precision=HI)
        spectral, row_sums = reduce_scatter(spectral, row_sums, "tm", 0)
        w_part = chunk_of(factor_w, "tm", 0)
        w_part = w_part * spectral / row_sums[None, :]
        factor_w = all_gather(w_part, "tm", 0)
    return (factor_w, factor_h)


def solution(mesh):
    in_specs = (P("tm"), P("freq", None), P(None, "tm"))
    out_specs = (P("freq", None), P(None, "tm"))
    return jax.shard_map(local, mesh=mesh, in_specs=in_specs, out_specs=out_specs, check_vma=False)
```

```python
import math

import functools

import jax
import jax.numpy as jnp
from jax import lax
from jax.experimental import pallas as pl
from jax.experimental.pallas import tpu as pltpu
from jax.sharding import PartitionSpec as P

WIN = 4096
HOP = 1024
K = 2048
ITERS = 2
HI = lax.Precision.HIGHEST


def shifted(value, axis, by):
    size = lax.axis_size(axis)
    pairs = [(i, i + by) for i in range(size) if 0 <= i + by < size]
    return lax.ppermute(value, axis, pairs)


def hann_window():
    samples = jnp.arange(WIN, dtype=jnp.int32).astype(jnp.float32)
    return 0.5 - 0.5 * jnp.cos(samples * (2.0 * math.pi / WIN))


SUB = 128


def small_tables(first, count):
    bins = first + jnp.arange(count, dtype=jnp.int32)
    a = jnp.arange(WIN // SUB, dtype=jnp.int32)
    b = jnp.arange(SUB, dtype=jnp.int32)
    pa = (a[:, None] * SUB * bins[None, :]) % WIN
    pb = (b[:, None] * bins[None, :]) % WIN
    sc = 2.0 * math.pi / WIN
    ta = pa.astype(jnp.float32) * sc
    tb = pb.astype(jnp.float32) * sc
    return jnp.cos(ta), jnp.sin(ta), jnp.cos(tb), jnp.sin(tb)


def dft_kernel(sig_hbm, tail_ref, win_ref, ca_ref, sa_ref, cb_ref, sb_ref, out_ref,
               blocks, tab, acc_ref, sem, *, tf, count, frames):
    i = pl.program_id(0)

    @pl.when(i == 0)
    def _():
        copy = pltpu.make_async_copy(sig_hbm, blocks.at[pl.ds(0, frames), :], sem)
        copy.start()
        blocks[pl.ds(frames, 8), :] = tail_ref[...]
        cb = cb_ref[...]
        sb = sb_ref[...]
        for a in range(WIN // SUB):
            ca = ca_ref[a:a + 1, :]
            sa = sa_ref[a:a + 1, :]
            tab[pl.ds(a * SUB, SUB), pl.ds(0, count)] = (ca * cb - sa * sb).astype(jnp.bfloat16)
            tab[pl.ds(a * SUB, SUB), pl.ds(count, count)] = (sa * cb + ca * sb).astype(jnp.bfloat16)
        copy.wait()

    base = pl.multiple_of(i * tf, tf)
    rows = blocks[pl.ds(base, tf + 8), :]
    for j in range(WIN // HOP):
        x = (rows[j:j + tf, :] * win_ref[j:j + 1, :]).astype(jnp.bfloat16)
        part = jnp.dot(x, tab[pl.ds(j * HOP, HOP), :], preferred_element_type=jnp.float32)
        if j == 0:
            acc_ref[...] = part
        else:
            acc_ref[...] += part
    re = acc_ref[:, :count]
    im = acc_ref[:, count:]
    out_ref[...] = ((re * re + im * im) / (0.375 * WIN)).T


def power_kernel(sig2d, tail8, win4, tables, count, tf=512, interpret=False):
    frames = sig2d.shape[0]
    ca, sa, cb, sb = tables
    full = lambda shape: pl.BlockSpec(shape, lambda i: (0, 0), pipeline_mode=pl.Buffered(1))
    return pl.pallas_call(
        functools.partial(dft_kernel, tf=tf, count=count, frames=frames),
        grid=(frames // tf,),
        in_specs=[pl.BlockSpec(memory_space=pl.ANY),
                  full(tail8.shape), full(win4.shape), full(ca.shape), full(sa.shape),
                  full(cb.shape), full(sb.shape)],
        out_specs=pl.BlockSpec((count, tf), lambda i: (0, i)),
        out_shape=jax.ShapeDtypeStruct((count, frames), jnp.float32),
        scratch_shapes=[pltpu.VMEM((frames + 8, HOP), jnp.float32),
                        pltpu.VMEM((WIN, 2 * count), jnp.bfloat16),
                        pltpu.VMEM((tf, 2 * count), jnp.float32),
                        pltpu.SemaphoreType.DMA],
        compiler_params=pltpu.CompilerParams(vmem_limit_bytes=48 * 1024 * 1024,
                                             dimension_semantics=("arbitrary",)),
        interpret=interpret,
    )(sig2d, tail8, win4, ca, sa, cb, sb)


def halves(x, dim, bit):
    lo, hi = jnp.split(x, 2, axis=dim)
    keep = jnp.where(bit == 0, lo, hi)
    send = jnp.where(bit == 0, hi, lo)
    return keep, send


def butterfly_rs(x, axis, dim):
    n = lax.axis_size(axis)
    idx = lax.axis_index(axis)
    d = 1
    while d < n:
        bit = (idx // d) % 2
        keep, send = halves(x, dim, bit)
        pairs = [(i, i ^ d) for i in range(n)]
        x = keep + lax.ppermute(send, axis, pairs)
        d *= 2
    return x


def butterfly_ag(x, axis, dim):
    n = lax.axis_size(axis)
    idx = lax.axis_index(axis)
    d = n // 2
    while d >= 1:
        bit = (idx // d) % 2
        pairs = [(i, i ^ d) for i in range(n)]
        got = lax.ppermute(x, axis, pairs)
        first = jnp.where(bit == 0, x, got)
        second = jnp.where(bit == 0, got, x)
        x = jnp.concatenate([first, second], axis=dim)
        d //= 2
    return x


def direct_rs(x, axis):
    n = lax.axis_size(axis)
    idx = lax.axis_index(axis)
    total = lax.dynamic_index_in_dim(x, idx, 0, keepdims=False)
    for s in range(1, n):
        part = lax.dynamic_index_in_dim(x, (idx + s) % n, 0, keepdims=False)
        total = total + lax.ppermute(part, axis, [(i, (i + s) % n) for i in range(n)])
    return total


def direct_ag(x, axis):
    n = lax.axis_size(axis)
    idx = lax.axis_index(axis)
    full = jnp.zeros((n,) + x.shape, x.dtype)
    full = lax.dynamic_update_index_in_dim(full, x, idx, 0)
    for s in range(1, n):
        got = lax.ppermute(x, axis, [(i, (i + s) % n) for i in range(n)])
        full = lax.dynamic_update_index_in_dim(full, got, (idx - s) % n, 0)
    return full


def local(signal, w_init, h_init):
    steps_per = WIN // HOP
    frames_dev = signal.shape[0] // HOP
    tail = shifted(signal[: (steps_per - 1) * HOP], "tm", -1)
    tail8 = jnp.concatenate([tail, jnp.zeros(((8 - steps_per + 1) * HOP,), jnp.float32)])
    local_bins = K // lax.axis_size("freq")
    win4 = hann_window().reshape(steps_per, HOP)
    tables = small_tables(lax.axis_index("freq") * local_bins, local_bins)
    power = power_kernel(signal.reshape(frames_dev, HOP), tail8.reshape(8, HOP), win4, tables, local_bins)
    factor_w = w_init
    factor_h = h_init
    rank = factor_w.shape[1]
    for step in range(ITERS):
        model = jnp.dot(factor_w, factor_h, precision=HI, preferred_element_type=jnp.float32)
        ratio = power / model
        numer = jnp.einsum("kr,kf->rf", factor_w, ratio, precision=HI)
        column_sums = jnp.sum(factor_w, axis=0)
        side = jnp.zeros((8, numer.shape[1]), jnp.float32).at[0, :rank].set(column_sums)
        both = butterfly_ag(butterfly_rs(jnp.concatenate([numer, side]), "freq", 1), "freq", 1)
        factor_h = factor_h * both[:rank] / both[rank, :rank][:, None]
        model = jnp.dot(factor_w, factor_h, precision=HI, preferred_element_type=jnp.float32)
        ratio = power / model
        row_sums = jnp.sum(factor_h, axis=1)
        spectral = jnp.einsum("kf,rf->kr", ratio, factor_h, precision=HI)
        n_tm = lax.axis_size("tm")
        chunks = spectral.reshape(n_tm, spectral.shape[0] // n_tm, rank)
        side = jnp.zeros((n_tm, 8, rank), jnp.float32).at[0, 0].set(row_sums)
        both = direct_ag(direct_rs(jnp.concatenate([chunks, side], axis=1), "tm"), "tm")
        spectral = both[:, :-8].reshape(spectral.shape)
        factor_w = factor_w * spectral / both[0, -8][None, :]
    return (factor_w, factor_h)


def solution(mesh):
    in_specs = (P("tm"), P("freq", None), P(None, "tm"))
    out_specs = (P("freq", None), P(None, "tm"))
    return jax.shard_map(local, mesh=mesh, in_specs=in_specs, out_specs=out_specs, check_vma=False)
```

```python
import math

import functools

import jax
import jax.numpy as jnp
from jax import lax
from jax.experimental import pallas as pl
from jax.experimental.pallas import tpu as pltpu
from jax.sharding import PartitionSpec as P

WIN = 4096
HOP = 1024
K = 2048
ITERS = 2
HI = lax.Precision.HIGH


def shifted(value, axis, by):
    size = lax.axis_size(axis)
    pairs = [(i, i + by) for i in range(size) if 0 <= i + by < size]
    return lax.ppermute(value, axis, pairs)


def hann_window():
    samples = jnp.arange(WIN, dtype=jnp.int32).astype(jnp.float32)
    return 0.5 - 0.5 * jnp.cos(samples * (2.0 * math.pi / WIN))


SUB = 128
LANES = HOP // 128


def small_tables(first, count):
    bins = first + jnp.arange(count, dtype=jnp.int32)
    a = jnp.arange(WIN // SUB, dtype=jnp.int32)
    b = jnp.arange(SUB, dtype=jnp.int32)
    pa = (a[:, None] * SUB * bins[None, :]) % WIN
    pb = (b[:, None] * bins[None, :]) % WIN
    sc = 2.0 * math.pi / WIN
    ta = pa.astype(jnp.float32) * sc
    tb = pb.astype(jnp.float32) * sc
    return jnp.cos(ta), jnp.sin(ta), jnp.cos(tb), jnp.sin(tb)


def dft_kernel(sig_hbm, tail_ref, win_ref, ca_ref, sa_ref, cb_ref, sb_ref, out_ref,
               blocks, tab, acc_ref, sem, *, tf, count, frames):
    i = pl.program_id(0)

    @pl.when(i == 0)
    def _():
        copy = pltpu.make_async_copy(sig_hbm, blocks.at[pl.ds(0, frames * LANES), :], sem)
        copy.start()
        blocks[pl.ds(frames * LANES, tail_ref.shape[0]), :] = tail_ref[...]
        cb = cb_ref[...]
        sb = sb_ref[...]
        for a in range(WIN // SUB):
            ca = ca_ref[a:a + 1, :]
            sa = sa_ref[a:a + 1, :]
            tab[pl.ds(a * SUB, SUB), pl.ds(0, count)] = (ca * cb - sa * sb).astype(jnp.bfloat16)
            tab[pl.ds(a * SUB, SUB), pl.ds(count, count)] = (sa * cb + ca * sb).astype(jnp.bfloat16)
        copy.wait()

    base = i * tf
    for j in range(WIN // HOP):
        pieces = [blocks[pl.ds((base + j) * LANES + u, tf, stride=LANES), :] for u in range(LANES)]
        x = (jnp.concatenate(pieces, axis=1) * win_ref[j:j + 1, :]).astype(jnp.bfloat16)
        part = jnp.dot(x, tab[pl.ds(j * HOP, HOP), :], preferred_element_type=jnp.float32)
        if j == 0:
            acc_ref[...] = part
        else:
            acc_ref[...] += part
    re = acc_ref[:, :count]
    im = acc_ref[:, count:]
    out_ref[...] = ((re * re + im * im) / (0.375 * WIN)).T


def power_kernel(sig2d, tail8, win4, tables, count, tf=512, interpret=False):
    frames = sig2d.shape[0] // LANES
    ca, sa, cb, sb = tables
    full = lambda shape: pl.BlockSpec(shape, lambda i: (0, 0), pipeline_mode=pl.Buffered(1))
    return pl.pallas_call(
        functools.partial(dft_kernel, tf=tf, count=count, frames=frames),
        grid=(frames // tf,),
        in_specs=[pl.BlockSpec(memory_space=pl.ANY),
                  full(tail8.shape), full(win4.shape), full(ca.shape), full(sa.shape),
                  full(cb.shape), full(sb.shape)],
        out_specs=pl.BlockSpec((count, tf), lambda i: (0, i)),
        out_shape=jax.ShapeDtypeStruct((count, frames), jnp.float32),
        scratch_shapes=[pltpu.VMEM((frames * LANES + tail8.shape[0], 128), jnp.float32),
                        pltpu.VMEM((WIN, 2 * count), jnp.bfloat16),
                        pltpu.VMEM((tf, 2 * count), jnp.float32),
                        pltpu.SemaphoreType.DMA],
        compiler_params=pltpu.CompilerParams(vmem_limit_bytes=48 * 1024 * 1024,
                                             dimension_semantics=("arbitrary",)),
        interpret=interpret,
    )(sig2d, tail8, win4, ca, sa, cb, sb)


def halves(x, dim, bit):
    lo, hi = jnp.split(x, 2, axis=dim)
    keep = jnp.where(bit == 0, lo, hi)
    send = jnp.where(bit == 0, hi, lo)
    return keep, send


def butterfly_rs(x, axis, dim):
    n = lax.axis_size(axis)
    idx = lax.axis_index(axis)
    d = 1
    while d < n:
        bit = (idx // d) % 2
        keep, send = halves(x, dim, bit)
        pairs = [(i, i ^ d) for i in range(n)]
        x = keep + lax.ppermute(send, axis, pairs)
        d *= 2
    return x


def butterfly_ag(x, axis, dim):
    n = lax.axis_size(axis)
    idx = lax.axis_index(axis)
    d = n // 2
    while d >= 1:
        bit = (idx // d) % 2
        pairs = [(i, i ^ d) for i in range(n)]
        got = lax.ppermute(x, axis, pairs)
        first = jnp.where(bit == 0, x, got)
        second = jnp.where(bit == 0, got, x)
        x = jnp.concatenate([first, second], axis=dim)
        d //= 2
    return x


def direct_rs(x, axis):
    n = lax.axis_size(axis)
    idx = lax.axis_index(axis)
    total = lax.dynamic_index_in_dim(x, idx, 0, keepdims=False)
    for s in range(1, n):
        part = lax.dynamic_index_in_dim(x, (idx + s) % n, 0, keepdims=False)
        total = total + lax.ppermute(part, axis, [(i, (i + s) % n) for i in range(n)])
    return total


def direct_ag(x, axis):
    n = lax.axis_size(axis)
    idx = lax.axis_index(axis)
    full = jnp.zeros((n,) + x.shape, x.dtype)
    full = lax.dynamic_update_index_in_dim(full, x, idx, 0)
    for s in range(1, n):
        got = lax.ppermute(x, axis, [(i, (i + s) % n) for i in range(n)])
        full = lax.dynamic_update_index_in_dim(full, got, (idx - s) % n, 0)
    return full


def local(signal, w_init, h_init):
    steps_per = WIN // HOP
    frames_dev = signal.shape[0] // HOP
    tail = shifted(signal[: (steps_per - 1) * HOP], "tm", -1)
    lanes = HOP // 128
    tail = tail.reshape((steps_per - 1) * lanes, 128)
    local_bins = K // lax.axis_size("freq")
    win4 = hann_window().reshape(steps_per, HOP)
    tables = small_tables(lax.axis_index("freq") * local_bins, local_bins)
    power = power_kernel(signal.reshape(frames_dev * lanes, 128), tail, win4, tables, local_bins)
    factor_w = w_init
    factor_h = h_init
    rank = factor_w.shape[1]
    for step in range(ITERS):
        model = jnp.dot(factor_w, factor_h, precision=HI, preferred_element_type=jnp.float32)
        ratio = power / model
        numer = jnp.einsum("kr,kf->rf", factor_w, ratio, precision=HI)
        column_sums = jnp.sum(factor_w, axis=0)
        side = jnp.zeros((8, numer.shape[1]), jnp.float32).at[0, :rank].set(column_sums)
        both = butterfly_ag(butterfly_rs(jnp.concatenate([numer, side]), "freq", 1), "freq", 1)
        factor_h = factor_h * both[:rank] / both[rank, :rank][:, None]
        model = jnp.dot(factor_w, factor_h, precision=HI, preferred_element_type=jnp.float32)
        ratio = power / model
        row_sums = jnp.sum(factor_h, axis=1)
        spectral = jnp.einsum("kf,rf->kr", ratio, factor_h, precision=HI)
        n_tm = lax.axis_size("tm")
        chunks = spectral.reshape(n_tm, spectral.shape[0] // n_tm, rank)
        side = jnp.zeros((n_tm, 8, rank), jnp.float32).at[0, 0].set(row_sums)
        both = direct_ag(direct_rs(jnp.concatenate([chunks, side], axis=1), "tm"), "tm")
        spectral = both[:, :-8].reshape(spectral.shape)
        factor_w = factor_w * spectral / both[0, -8][None, :]
    return (factor_w, factor_h)


def solution(mesh):
    in_specs = (P("tm"), P("freq", None), P(None, "tm"))
    out_specs = (P("freq", None), P(None, "tm"))
    return jax.shard_map(local, mesh=mesh, in_specs=in_specs, out_specs=out_specs, check_vma=False)
```

```python
import math

import functools

import jax
import jax.numpy as jnp
from jax import lax
from jax.experimental import pallas as pl
from jax.experimental.pallas import tpu as pltpu
from jax.sharding import PartitionSpec as P

WIN = 4096
HOP = 1024
K = 2048
ITERS = 2
HI = lax.Precision.HIGH


def shifted(value, axis, by):
    size = lax.axis_size(axis)
    pairs = [(i, i + by) for i in range(size) if 0 <= i + by < size]
    return lax.ppermute(value, axis, pairs)


def hann_window():
    samples = jnp.arange(WIN, dtype=jnp.int32).astype(jnp.float32)
    return 0.5 - 0.5 * jnp.cos(samples * (2.0 * math.pi / WIN))


SUB = 128
LANES = HOP // 128


def small_tables(first, count):
    bins = first + jnp.arange(count, dtype=jnp.int32)
    a = jnp.arange(WIN // SUB, dtype=jnp.int32)
    b = jnp.arange(SUB, dtype=jnp.int32)
    pa = (a[:, None] * SUB * bins[None, :]) % WIN
    pb = (b[:, None] * bins[None, :]) % WIN
    sc = 2.0 * math.pi / WIN
    ta = pa.astype(jnp.float32) * sc
    tb = pb.astype(jnp.float32) * sc
    return jnp.cos(ta), jnp.sin(ta), jnp.cos(tb), jnp.sin(tb)


def dft_kernel(sig_hbm, tail_ref, win_ref, ca_ref, sa_ref, cb_ref, sb_ref, out_ref,
               blocks, tab, acc_ref, sem, *, tf, count, frames):
    i = pl.program_id(0)

    @pl.when(i == 0)
    def _():
        copy = pltpu.make_async_copy(sig_hbm, blocks.at[pl.ds(0, frames * LANES), :], sem)
        copy.start()
        blocks[pl.ds(frames * LANES, tail_ref.shape[0]), :] = tail_ref[...]
        cb = cb_ref[...]
        sb = sb_ref[...]
        for a in range(WIN // SUB):
            ca = ca_ref[a:a + 1, :]
            sa = sa_ref[a:a + 1, :]
            tab[pl.ds(a * SUB, SUB), pl.ds(0, count)] = (ca * cb - sa * sb).astype(jnp.bfloat16)
            tab[pl.ds(a * SUB, SUB), pl.ds(count, count)] = (sa * cb + ca * sb).astype(jnp.bfloat16)
        copy.wait()

    base = i * tf
    for j in range(WIN // HOP):
        pieces = [blocks[pl.ds((base + j) * LANES + u, tf, stride=LANES), :] for u in range(LANES)]
        x = (jnp.concatenate(pieces, axis=1) * win_ref[j:j + 1, :]).astype(jnp.bfloat16)
        part = jnp.dot(x, tab[pl.ds(j * HOP, HOP), :], preferred_element_type=jnp.float32)
        if j == 0:
            acc_ref[...] = part
        else:
            acc_ref[...] += part
    re = acc_ref[:, :count]
    im = acc_ref[:, count:]
    out_ref[...] = ((re * re + im * im) / (0.375 * WIN)).T


def power_kernel(sig2d, tail8, win4, tables, count, tf=512, interpret=False):
    frames = sig2d.shape[0] // LANES
    ca, sa, cb, sb = tables
    full = lambda shape: pl.BlockSpec(shape, lambda i: (0, 0), pipeline_mode=pl.Buffered(1))
    return pl.pallas_call(
        functools.partial(dft_kernel, tf=tf, count=count, frames=frames),
        grid=(frames // tf,),
        in_specs=[pl.BlockSpec(memory_space=pl.ANY),
                  full(tail8.shape), full(win4.shape), full(ca.shape), full(sa.shape),
                  full(cb.shape), full(sb.shape)],
        out_specs=pl.BlockSpec((count, tf), lambda i: (0, i)),
        out_shape=jax.ShapeDtypeStruct((count, frames), jnp.float32),
        scratch_shapes=[pltpu.VMEM((frames * LANES + tail8.shape[0], 128), jnp.float32),
                        pltpu.VMEM((WIN, 2 * count), jnp.bfloat16),
                        pltpu.VMEM((tf, 2 * count), jnp.float32),
                        pltpu.SemaphoreType.DMA],
        compiler_params=pltpu.CompilerParams(vmem_limit_bytes=48 * 1024 * 1024,
                                             dimension_semantics=("arbitrary",)),
        interpret=interpret,
    )(sig2d, tail8, win4, ca, sa, cb, sb)


def halves(x, dim, bit):
    lo, hi = jnp.split(x, 2, axis=dim)
    keep = jnp.where(bit == 0, lo, hi)
    send = jnp.where(bit == 0, hi, lo)
    return keep, send


def butterfly_rs(x, axis, dim):
    n = lax.axis_size(axis)
    idx = lax.axis_index(axis)
    d = 1
    while d < n:
        bit = (idx // d) % 2
        keep, send = halves(x, dim, bit)
        pairs = [(i, i ^ d) for i in range(n)]
        x = keep + lax.ppermute(send, axis, pairs)
        d *= 2
    return x


def butterfly_ag(x, axis, dim):
    n = lax.axis_size(axis)
    idx = lax.axis_index(axis)
    d = n // 2
    while d >= 1:
        bit = (idx // d) % 2
        pairs = [(i, i ^ d) for i in range(n)]
        got = lax.ppermute(x, axis, pairs)
        first = jnp.where(bit == 0, x, got)
        second = jnp.where(bit == 0, got, x)
        x = jnp.concatenate([first, second], axis=dim)
        d //= 2
    return x


def pairs_of(n, stride, s):
    m = n // stride
    return [(i, ((i // stride + s) % m) * stride + i % stride) for i in range(n)]


def direct_rs(x, axis, stride=1):
    n = lax.axis_size(axis)
    m = n // stride
    g = lax.axis_index(axis) // stride
    xr = jnp.roll(x, -g, axis=0)
    total = xr[0]
    for s in range(1, m):
        total = total + lax.ppermute(xr[s], axis, pairs_of(n, stride, s))
    return total


def direct_ag(x, axis, stride=1):
    n = lax.axis_size(axis)
    m = n // stride
    g = lax.axis_index(axis) // stride
    got = [x] + [lax.ppermute(x, axis, pairs_of(n, stride, s)) for s in range(1, m)]
    rev = jnp.stack([got[(m - t) % m] for t in range(m)])
    return jnp.roll(rev, g, axis=0)


def pair_rs(x, axis):
    n = lax.axis_size(axis)
    bit = lax.axis_index(axis) % 2
    x = x.reshape((n // 2, 2) + x.shape[1:])
    keep = jnp.where(bit == 0, x[:, 0], x[:, 1])
    send = jnp.where(bit == 0, x[:, 1], x[:, 0])
    x = keep + lax.ppermute(send, axis, [(i, i ^ 1) for i in range(n)])
    return direct_rs(x, axis, 2)


def pair_ag(x, axis):
    n = lax.axis_size(axis)
    bit = lax.axis_index(axis) % 2
    x = direct_ag(x, axis, 2)
    got = lax.ppermute(x, axis, [(i, i ^ 1) for i in range(n)])
    first = jnp.where(bit == 0, x, got)
    second = jnp.where(bit == 0, got, x)
    return jnp.stack([first, second], axis=1).reshape((n,) + x.shape[1:])


def local(signal, w_init, h_init):
    steps_per = WIN // HOP
    frames_dev = signal.shape[0] // HOP
    tail = shifted(signal[: (steps_per - 1) * HOP], "tm", -1)
    lanes = HOP // 128
    tail = tail.reshape((steps_per - 1) * lanes, 128)
    local_bins = K // lax.axis_size("freq")
    win4 = hann_window().reshape(steps_per, HOP)
    tables = small_tables(lax.axis_index("freq") * local_bins, local_bins)
    power = power_kernel(signal.reshape(frames_dev * lanes, 128), tail, win4, tables, local_bins)
    factor_w = w_init
    factor_h = h_init
    rank = factor_w.shape[1]
    for step in range(ITERS):
        model = jnp.dot(factor_w, factor_h, precision=HI, preferred_element_type=jnp.float32)
        ratio = power / model
        numer = jnp.einsum("kr,kf->rf", factor_w, ratio, precision=HI)
        column_sums = jnp.sum(factor_w, axis=0)
        side = jnp.zeros((8, numer.shape[1]), jnp.float32).at[0, :rank].set(column_sums)
        both = butterfly_ag(butterfly_rs(jnp.concatenate([numer, side]), "freq", 1), "freq", 1)
        factor_h = factor_h * both[:rank] / both[rank, :rank][:, None]
        model = jnp.dot(factor_w, factor_h, precision=HI, preferred_element_type=jnp.float32)
        ratio = power / model
        row_sums = jnp.sum(factor_h, axis=1)
        spectral = jnp.einsum("kf,rf->kr", ratio, factor_h, precision=HI)
        n_tm = lax.axis_size("tm")
        chunks = spectral.reshape(n_tm, spectral.shape[0] // n_tm, rank)
        side = jnp.zeros((n_tm, 8, rank), jnp.float32).at[0, 0].set(row_sums)
        both = pair_ag(pair_rs(jnp.concatenate([chunks, side], axis=1), "tm"), "tm")
        spectral = both[:, :-8].reshape(spectral.shape)
        factor_w = factor_w * spectral / both[0, -8][None, :]
    return (factor_w, factor_h)


def solution(mesh):
    in_specs = (P("tm"), P("freq", None), P(None, "tm"))
    out_specs = (P("freq", None), P(None, "tm"))
    return jax.shard_map(local, mesh=mesh, in_specs=in_specs, out_specs=out_specs, check_vma=False)
```

```python
import math

import functools

import jax
import jax.numpy as jnp
from jax import lax
from jax.experimental import pallas as pl
from jax.experimental.pallas import tpu as pltpu
from jax.sharding import PartitionSpec as P

WIN = 4096
HOP = 1024
K = 2048
ITERS = 2
HI = lax.Precision.HIGH


def shifted(value, axis, by):
    size = lax.axis_size(axis)
    pairs = [(i, i + by) for i in range(size) if 0 <= i + by < size]
    return lax.ppermute(value, axis, pairs)


def hann_window():
    samples = jnp.arange(WIN, dtype=jnp.int32).astype(jnp.float32)
    return 0.5 - 0.5 * jnp.cos(samples * (2.0 * math.pi / WIN))


SUB = 128
LANES = HOP // 128


def small_tables(first, count):
    bins = first + jnp.arange(count, dtype=jnp.int32)
    a = jnp.arange(WIN // SUB, dtype=jnp.int32)
    b = jnp.arange(SUB, dtype=jnp.int32)
    pa = (a[:, None] * SUB * bins[None, :]) % WIN
    pb = (b[:, None] * bins[None, :]) % WIN
    sc = 2.0 * math.pi / WIN
    ta = pa.astype(jnp.float32) * sc
    tb = pb.astype(jnp.float32) * sc
    return jnp.cos(ta), jnp.sin(ta), jnp.cos(tb), jnp.sin(tb)


def dft_kernel(sig_hbm, tail_ref, win_ref, ca_ref, sa_ref, cb_ref, sb_ref, out_ref,
               blocks, tab, acc_ref, sem, *, tf, count, frames):
    i = pl.program_id(0)

    @pl.when(i == 0)
    def _():
        copy = pltpu.make_async_copy(sig_hbm, blocks.at[pl.ds(0, frames * LANES), :], sem)
        copy.start()
        blocks[pl.ds(frames * LANES, tail_ref.shape[0]), :] = tail_ref[...]
        cb = cb_ref[...]
        sb = sb_ref[...]
        for a in range(WIN // SUB):
            ca = ca_ref[a:a + 1, :]
            sa = sa_ref[a:a + 1, :]
            tab[pl.ds(a * SUB, SUB), pl.ds(0, count)] = (ca * cb - sa * sb).astype(jnp.bfloat16)
            tab[pl.ds(a * SUB, SUB), pl.ds(count, count)] = (sa * cb + ca * sb).astype(jnp.bfloat16)
        copy.wait()

    base = i * tf
    for j in range(WIN // HOP):
        pieces = [blocks[pl.ds((base + j) * LANES + u, tf, stride=LANES), :] for u in range(LANES)]
        x = (jnp.concatenate(pieces, axis=1) * win_ref[j:j + 1, :]).astype(jnp.bfloat16)
        part = jnp.dot(x, tab[pl.ds(j * HOP, HOP), :], preferred_element_type=jnp.float32)
        if j == 0:
            acc_ref[...] = part
        else:
            acc_ref[...] += part
    re = acc_ref[:, :count]
    im = acc_ref[:, count:]
    out_ref[...] = ((re * re + im * im) / (0.375 * WIN)).T


def power_kernel(sig2d, tail8, win4, tables, count, tf=512, interpret=False):
    frames = sig2d.shape[0] // LANES
    ca, sa, cb, sb = tables
    full = lambda shape: pl.BlockSpec(shape, lambda i: (0, 0), pipeline_mode=pl.Buffered(1))
    return pl.pallas_call(
        functools.partial(dft_kernel, tf=tf, count=count, frames=frames),
        grid=(frames // tf,),
        in_specs=[pl.BlockSpec(memory_space=pl.ANY),
                  full(tail8.shape), full(win4.shape), full(ca.shape), full(sa.shape),
                  full(cb.shape), full(sb.shape)],
        out_specs=pl.BlockSpec((count, tf), lambda i: (0, i)),
        out_shape=jax.ShapeDtypeStruct((count, frames), jnp.float32),
        scratch_shapes=[pltpu.VMEM((frames * LANES + tail8.shape[0], 128), jnp.float32),
                        pltpu.VMEM((WIN, 2 * count), jnp.bfloat16),
                        pltpu.VMEM((tf, 2 * count), jnp.float32),
                        pltpu.SemaphoreType.DMA],
        compiler_params=pltpu.CompilerParams(vmem_limit_bytes=48 * 1024 * 1024,
                                             dimension_semantics=("arbitrary",)),
        interpret=interpret,
    )(sig2d, tail8, win4, ca, sa, cb, sb)


def halves(x, dim, bit):
    lo, hi = jnp.split(x, 2, axis=dim)
    keep = jnp.where(bit == 0, lo, hi)
    send = jnp.where(bit == 0, hi, lo)
    return keep, send


def butterfly_rs(x, axis, dim):
    n = lax.axis_size(axis)
    idx = lax.axis_index(axis)
    d = 1
    while d < n:
        bit = (idx // d) % 2
        keep, send = halves(x, dim, bit)
        pairs = [(i, i ^ d) for i in range(n)]
        x = keep + lax.ppermute(send, axis, pairs)
        d *= 2
    return x


def butterfly_ag(x, axis, dim):
    n = lax.axis_size(axis)
    idx = lax.axis_index(axis)
    d = n // 2
    while d >= 1:
        bit = (idx // d) % 2
        pairs = [(i, i ^ d) for i in range(n)]
        got = lax.ppermute(x, axis, pairs)
        first = jnp.where(bit == 0, x, got)
        second = jnp.where(bit == 0, got, x)
        x = jnp.concatenate([first, second], axis=dim)
        d //= 2
    return x


def pairs_of(n, stride, s):
    m = n // stride
    return [(i, ((i // stride + s) % m) * stride + i % stride) for i in range(n)]


def direct_rs(x, axis, stride=1):
    n = lax.axis_size(axis)
    m = n // stride
    g = lax.axis_index(axis) // stride
    xr = jnp.roll(x, -g, axis=0)
    total = xr[0]
    for s in range(1, m):
        total = total + lax.ppermute(xr[s], axis, pairs_of(n, stride, s))
    return total


def direct_ag(x, axis, stride=1):
    n = lax.axis_size(axis)
    m = n // stride
    g = lax.axis_index(axis) // stride
    got = [x] + [lax.ppermute(x, axis, pairs_of(n, stride, s)) for s in range(1, m)]
    rev = jnp.stack([got[(m - t) % m] for t in range(m)])
    return jnp.roll(rev, g, axis=0)


def pair_step(x, axis):
    n = lax.axis_size(axis)
    bit = lax.axis_index(axis) % 2
    x = x.reshape((n // 2, 2) + x.shape[1:])
    keep = jnp.where(bit == 0, x[:, 0], x[:, 1])
    send = jnp.where(bit == 0, x[:, 1], x[:, 0])
    return keep + lax.ppermute(send, axis, [(i, i ^ 1) for i in range(n)])


def pair_gather(x, axis):
    n = lax.axis_size(axis)
    bit = lax.axis_index(axis) % 2
    got = lax.ppermute(x, axis, [(i, i ^ 1) for i in range(n)])
    first = jnp.where(bit == 0, x, got)
    second = jnp.where(bit == 0, got, x)
    return jnp.stack([first, second], axis=1).reshape((n,) + x.shape[1:])


def piped_all_reduce(x, axis):
    half = x.shape[-1] // 2
    a, b = x[..., :half], x[..., half:]
    a = pair_step(a, axis)
    b, a = lax.optimization_barrier((b, a))
    a = direct_rs(a, axis, 2)
    b = pair_step(b, axis)
    b, a = lax.optimization_barrier((b, a))
    b = direct_rs(b, axis, 2)
    a = direct_ag(a, axis, 2)
    b, a = lax.optimization_barrier((b, a))
    a = pair_gather(a, axis)
    b = direct_ag(b, axis, 2)
    b, a = lax.optimization_barrier((b, a))
    b = pair_gather(b, axis)
    return jnp.concatenate([a, b], axis=-1)


def local(signal, w_init, h_init):
    steps_per = WIN // HOP
    frames_dev = signal.shape[0] // HOP
    tail = shifted(signal[: (steps_per - 1) * HOP], "tm", -1)
    lanes = HOP // 128
    tail = tail.reshape((steps_per - 1) * lanes, 128)
    local_bins = K // lax.axis_size("freq")
    win4 = hann_window().reshape(steps_per, HOP)
    tables = small_tables(lax.axis_index("freq") * local_bins, local_bins)
    power = power_kernel(signal.reshape(frames_dev * lanes, 128), tail, win4, tables, local_bins)
    factor_w = w_init
    factor_h = h_init
    rank = factor_w.shape[1]
    for step in range(ITERS):
        model = jnp.dot(factor_w, factor_h, precision=HI, preferred_element_type=jnp.float32)
        ratio = power / model
        numer = jnp.einsum("kr,kf->rf", factor_w, ratio, precision=HI)
        column_sums = jnp.sum(factor_w, axis=0)
        side = jnp.zeros((8, numer.shape[1]), jnp.float32).at[0, :rank].set(column_sums)
        both = butterfly_ag(butterfly_rs(jnp.concatenate([numer, side]), "freq", 1), "freq", 1)
        factor_h = factor_h * both[:rank] / both[rank, :rank][:, None]
        model = jnp.dot(factor_w, factor_h, precision=HI, preferred_element_type=jnp.float32)
        ratio = power / model
        row_sums = jnp.sum(factor_h, axis=1)
        spectral = jnp.einsum("kf,rf->kr", ratio, factor_h, precision=HI)
        n_tm = lax.axis_size("tm")
        chunks = spectral.reshape(n_tm, spectral.shape[0] // n_tm, rank)
        side = jnp.zeros((n_tm, 8, rank), jnp.float32).at[0, 0].set(row_sums)
        both = piped_all_reduce(jnp.concatenate([chunks, side], axis=1), "tm")
        spectral = both[:, :-8].reshape(spectral.shape)
        factor_w = factor_w * spectral / both[0, -8][None, :]
    return (factor_w, factor_h)


def solution(mesh):
    in_specs = (P("tm"), P("freq", None), P(None, "tm"))
    out_specs = (P("freq", None), P(None, "tm"))
    return jax.shard_map(local, mesh=mesh, in_specs=in_specs, out_specs=out_specs, check_vma=False)
```

```python
import math

import functools

import jax
import jax.numpy as jnp
from jax import lax
from jax.experimental import pallas as pl
from jax.experimental.pallas import tpu as pltpu
from jax.sharding import PartitionSpec as P

WIN = 4096
HOP = 1024
K = 2048
ITERS = 2
HI = lax.Precision.HIGH


def shifted(value, axis, by):
    size = lax.axis_size(axis)
    pairs = [(i, i + by) for i in range(size) if 0 <= i + by < size]
    return lax.ppermute(value, axis, pairs)


def hann_window():
    samples = jnp.arange(WIN, dtype=jnp.int32).astype(jnp.float32)
    return 0.5 - 0.5 * jnp.cos(samples * (2.0 * math.pi / WIN))


SUB = 128
LANES = HOP // 128


def small_tables(first, count):
    bins = first + jnp.arange(count, dtype=jnp.int32)
    a = jnp.arange(WIN // SUB, dtype=jnp.int32)
    b = jnp.arange(SUB, dtype=jnp.int32)
    pa = (a[:, None] * SUB * bins[None, :]) % WIN
    pb = (b[:, None] * bins[None, :]) % WIN
    sc = 2.0 * math.pi / WIN
    ta = pa.astype(jnp.float32) * sc
    tb = pb.astype(jnp.float32) * sc
    return jnp.cos(ta), jnp.sin(ta), jnp.cos(tb), jnp.sin(tb)


def dft_kernel(sig_hbm, tail_ref, win_ref, ca_ref, sa_ref, cb_ref, sb_ref, out_ref,
               blocks, tab, acc_ref, sem, *, tf, count, frames):
    i = pl.program_id(0)

    @pl.when(i == 0)
    def _():
        copy = pltpu.make_async_copy(sig_hbm, blocks.at[pl.ds(0, frames * LANES), :], sem)
        copy.start()
        blocks[pl.ds(frames * LANES, tail_ref.shape[0]), :] = tail_ref[...]
        cb = cb_ref[...]
        sb = sb_ref[...]
        for a in range(WIN // SUB):
            ca = ca_ref[a:a + 1, :]
            sa = sa_ref[a:a + 1, :]
            tab[pl.ds(a * SUB, SUB), pl.ds(0, count)] = (ca * cb - sa * sb).astype(jnp.bfloat16)
            tab[pl.ds(a * SUB, SUB), pl.ds(count, count)] = (sa * cb + ca * sb).astype(jnp.bfloat16)
        copy.wait()

    base = i * tf
    for j in range(WIN // HOP):
        pieces = [blocks[pl.ds((base + j) * LANES + u, tf, stride=LANES), :] for u in range(LANES)]
        x = (jnp.concatenate(pieces, axis=1) * win_ref[j:j + 1, :]).astype(jnp.bfloat16)
        part = jnp.dot(x, tab[pl.ds(j * HOP, HOP), :], preferred_element_type=jnp.float32)
        if j == 0:
            acc_ref[...] = part
        else:
            acc_ref[...] += part
    re = acc_ref[:, :count]
    im = acc_ref[:, count:]
    out_ref[...] = ((re * re + im * im) / (0.375 * WIN)).T


def power_kernel(sig2d, tail8, win4, tables, count, tf=512, interpret=False):
    frames = sig2d.shape[0] // LANES
    ca, sa, cb, sb = tables
    full = lambda shape: pl.BlockSpec(shape, lambda i: (0, 0), pipeline_mode=pl.Buffered(1))
    return pl.pallas_call(
        functools.partial(dft_kernel, tf=tf, count=count, frames=frames),
        grid=(frames // tf,),
        in_specs=[pl.BlockSpec(memory_space=pl.ANY),
                  full(tail8.shape), full(win4.shape), full(ca.shape), full(sa.shape),
                  full(cb.shape), full(sb.shape)],
        out_specs=pl.BlockSpec((count, tf), lambda i: (0, i)),
        out_shape=jax.ShapeDtypeStruct((count, frames), jnp.float32),
        scratch_shapes=[pltpu.VMEM((frames * LANES + tail8.shape[0], 128), jnp.float32),
                        pltpu.VMEM((WIN, 2 * count), jnp.bfloat16),
                        pltpu.VMEM((tf, 2 * count), jnp.float32),
                        pltpu.SemaphoreType.DMA],
        compiler_params=pltpu.CompilerParams(vmem_limit_bytes=48 * 1024 * 1024,
                                             dimension_semantics=("arbitrary",)),
        interpret=interpret,
    )(sig2d, tail8, win4, ca, sa, cb, sb)


def halves(x, dim, bit):
    lo, hi = jnp.split(x, 2, axis=dim)
    keep = jnp.where(bit == 0, lo, hi)
    send = jnp.where(bit == 0, hi, lo)
    return keep, send


def butterfly_rs(x, axis, dim):
    n = lax.axis_size(axis)
    idx = lax.axis_index(axis)
    d = 1
    while d < n:
        bit = (idx // d) % 2
        keep, send = halves(x, dim, bit)
        pairs = [(i, i ^ d) for i in range(n)]
        x = keep + lax.ppermute(send, axis, pairs)
        d *= 2
    return x


def butterfly_ag(x, axis, dim):
    n = lax.axis_size(axis)
    idx = lax.axis_index(axis)
    d = n // 2
    while d >= 1:
        bit = (idx // d) % 2
        pairs = [(i, i ^ d) for i in range(n)]
        got = lax.ppermute(x, axis, pairs)
        first = jnp.where(bit == 0, x, got)
        second = jnp.where(bit == 0, got, x)
        x = jnp.concatenate([first, second], axis=dim)
        d //= 2
    return x


def pairs_of(n, stride, s):
    m = n // stride
    return [(i, ((i // stride + s) % m) * stride + i % stride) for i in range(n)]


def direct_rs(x, axis, stride=1):
    n = lax.axis_size(axis)
    m = n // stride
    g = lax.axis_index(axis) // stride
    xr = jnp.roll(x, -g, axis=0)
    total = xr[0]
    for s in range(1, m):
        total = total + lax.ppermute(xr[s], axis, pairs_of(n, stride, s))
    return total


def direct_ag(x, axis, stride=1):
    n = lax.axis_size(axis)
    m = n // stride
    g = lax.axis_index(axis) // stride
    got = [x] + [lax.ppermute(x, axis, pairs_of(n, stride, s)) for s in range(1, m)]
    rev = jnp.stack([got[(m - t) % m] for t in range(m)])
    return jnp.roll(rev, g, axis=0)


def pair_rs(x, axis):
    n = lax.axis_size(axis)
    bit = lax.axis_index(axis) % 2
    x = x.reshape((n // 2, 2) + x.shape[1:])
    keep = jnp.where(bit == 0, x[:, 0], x[:, 1])
    send = jnp.where(bit == 0, x[:, 1], x[:, 0])
    x = keep + lax.ppermute(send, axis, [(i, i ^ 1) for i in range(n)])
    return direct_rs(x, axis, 2)


def pair_ag(x, axis):
    n = lax.axis_size(axis)
    bit = lax.axis_index(axis) % 2
    x = direct_ag(x, axis, 2)
    got = lax.ppermute(x, axis, [(i, i ^ 1) for i in range(n)])
    first = jnp.where(bit == 0, x, got)
    second = jnp.where(bit == 0, got, x)
    return jnp.stack([first, second], axis=1).reshape((n,) + x.shape[1:])


def butterfly_all_reduce(x, axis, dim):
    n = lax.axis_size(axis)
    idx = lax.axis_index(axis)
    d = 1
    while d < n // 2:
        bit = (idx // d) % 2
        keep, send = halves(x, dim, bit)
        x = keep + lax.ppermute(send, axis, [(i, i ^ d) for i in range(n)])
        d *= 2
    x = x + lax.ppermute(x, axis, [(i, i ^ d) for i in range(n)])
    d //= 2
    while d >= 1:
        bit = (idx // d) % 2
        got = lax.ppermute(x, axis, [(i, i ^ d) for i in range(n)])
        first = jnp.where(bit == 0, x, got)
        second = jnp.where(bit == 0, got, x)
        x = jnp.concatenate([first, second], axis=dim)
        d //= 2
    return x


def z_then_pair(x, axis):
    n = lax.axis_size(axis)
    m = n // 2
    x = x.reshape((2, m) + x.shape[1:])
    x = jnp.moveaxis(x, 0, 1)
    x = direct_rs(x, axis, 2)
    x = x + lax.ppermute(x, axis, [(i, i ^ 1) for i in range(n)])
    x = direct_ag(x, axis, 2)
    return jnp.moveaxis(x, 1, 0).reshape((n,) + x.shape[2:])


def local(signal, w_init, h_init):
    steps_per = WIN // HOP
    frames_dev = signal.shape[0] // HOP
    tail = shifted(signal[: (steps_per - 1) * HOP], "tm", -1)
    lanes = HOP // 128
    tail = tail.reshape((steps_per - 1) * lanes, 128)
    local_bins = K // lax.axis_size("freq")
    win4 = hann_window().reshape(steps_per, HOP)
    tables = small_tables(lax.axis_index("freq") * local_bins, local_bins)
    power = power_kernel(signal.reshape(frames_dev * lanes, 128), tail, win4, tables, local_bins)
    factor_w = w_init
    factor_h = h_init
    rank = factor_w.shape[1]
    for step in range(ITERS):
        model = jnp.dot(factor_w, factor_h, precision=HI, preferred_element_type=jnp.float32)
        ratio = power / model
        numer = jnp.einsum("kr,kf->rf", factor_w, ratio, precision=HI)
        column_sums = jnp.sum(factor_w, axis=0)
        side = jnp.zeros((8, numer.shape[1]), jnp.float32).at[0, :rank].set(column_sums)
        both = butterfly_all_reduce(jnp.concatenate([numer, side]), "freq", 1)
        factor_h = factor_h * both[:rank] / both[rank, :rank][:, None]
        model = jnp.dot(factor_w, factor_h, precision=HI, preferred_element_type=jnp.float32)
        ratio = power / model
        row_sums = jnp.sum(factor_h, axis=1)
        spectral = jnp.einsum("kf,rf->kr", ratio, factor_h, precision=HI)
        n_tm = lax.axis_size("tm")
        chunks = spectral.reshape(n_tm, spectral.shape[0] // n_tm, rank)
        side = jnp.zeros((n_tm, 8, rank), jnp.float32).at[0, 0].set(row_sums)
        both = z_then_pair(jnp.concatenate([chunks, side], axis=1), "tm")
        spectral = both[:, :-8].reshape(spectral.shape)
        factor_w = factor_w * spectral / both[0, -8][None, :]
    return (factor_w, factor_h)


def solution(mesh):
    in_specs = (P("tm"), P("freq", None), P(None, "tm"))
    out_specs = (P("freq", None), P(None, "tm"))
    return jax.shard_map(local, mesh=mesh, in_specs=in_specs, out_specs=out_specs, check_vma=False)
```

```python
import math

import functools

import jax
import jax.numpy as jnp
from jax import lax
from jax.experimental import pallas as pl
from jax.experimental.pallas import tpu as pltpu
from jax.sharding import PartitionSpec as P

WIN = 4096
HOP = 1024
K = 2048
ITERS = 2
HI = lax.Precision.HIGH


def shifted(value, axis, by):
    size = lax.axis_size(axis)
    pairs = [(i, i + by) for i in range(size) if 0 <= i + by < size]
    return lax.ppermute(value, axis, pairs)


def hann_window():
    samples = jnp.arange(WIN, dtype=jnp.int32).astype(jnp.float32)
    return 0.5 - 0.5 * jnp.cos(samples * (2.0 * math.pi / WIN))


SUB = 128
LANES = HOP // 128


def small_tables(first, count):
    bins = first + jnp.arange(count, dtype=jnp.int32)
    a = jnp.arange(WIN // SUB, dtype=jnp.int32)
    b = jnp.arange(SUB, dtype=jnp.int32)
    pa = (a[:, None] * SUB * bins[None, :]) % WIN
    pb = (b[:, None] * bins[None, :]) % WIN
    sc = 2.0 * math.pi / WIN
    ta = pa.astype(jnp.float32) * sc
    tb = pb.astype(jnp.float32) * sc
    return jnp.cos(ta), jnp.sin(ta), jnp.cos(tb), jnp.sin(tb)


def dft_kernel(sig_hbm, tail_ref, win_ref, ca_ref, sa_ref, cb_ref, sb_ref, out_ref,
               blocks, tab, acc_ref, sem, *, tf, count, frames):
    i = pl.program_id(0)

    @pl.when(i == 0)
    def _():
        copy = pltpu.make_async_copy(sig_hbm, blocks.at[pl.ds(0, frames * LANES), :], sem)
        copy.start()
        blocks[pl.ds(frames * LANES, tail_ref.shape[0]), :] = tail_ref[...]
        cb = cb_ref[...]
        sb = sb_ref[...]
        for a in range(WIN // SUB):
            ca = ca_ref[a:a + 1, :]
            sa = sa_ref[a:a + 1, :]
            tab[pl.ds(a * SUB, SUB), pl.ds(0, count)] = (ca * cb - sa * sb).astype(jnp.bfloat16)
            tab[pl.ds(a * SUB, SUB), pl.ds(count, count)] = (sa * cb + ca * sb).astype(jnp.bfloat16)
        copy.wait()

    base = i * tf
    for j in range(WIN // HOP):
        pieces = [blocks[pl.ds((base + j) * LANES + u, tf, stride=LANES), :] for u in range(LANES)]
        x = (jnp.concatenate(pieces, axis=1) * win_ref[j:j + 1, :]).astype(jnp.bfloat16)
        part = jnp.dot(x, tab[pl.ds(j * HOP, HOP), :], preferred_element_type=jnp.float32)
        acc = part if j == 0 else acc + part
    re = acc[:, :count]
    im = acc[:, count:]
    out_ref[...] = ((re * re + im * im) / (0.375 * WIN)).T


def power_kernel(sig2d, tail8, win4, tables, count, tf=512, interpret=False):
    frames = sig2d.shape[0] // LANES
    ca, sa, cb, sb = tables
    full = lambda shape: pl.BlockSpec(shape, lambda i: (0, 0), pipeline_mode=pl.Buffered(1))
    return pl.pallas_call(
        functools.partial(dft_kernel, tf=tf, count=count, frames=frames),
        grid=(frames // tf,),
        in_specs=[pl.BlockSpec(memory_space=pl.ANY),
                  full(tail8.shape), full(win4.shape), full(ca.shape), full(sa.shape),
                  full(cb.shape), full(sb.shape)],
        out_specs=pl.BlockSpec((count, tf), lambda i: (0, i)),
        out_shape=jax.ShapeDtypeStruct((count, frames), jnp.float32),
        scratch_shapes=[pltpu.VMEM((frames * LANES + tail8.shape[0], 128), jnp.float32),
                        pltpu.VMEM((WIN, 2 * count), jnp.bfloat16),
                        pltpu.VMEM((tf, 2 * count), jnp.float32),
                        pltpu.SemaphoreType.DMA],
        compiler_params=pltpu.CompilerParams(vmem_limit_bytes=48 * 1024 * 1024,
                                             dimension_semantics=("arbitrary",)),
        interpret=interpret,
    )(sig2d, tail8, win4, ca, sa, cb, sb)


def halves(x, dim, bit):
    lo, hi = jnp.split(x, 2, axis=dim)
    keep = jnp.where(bit == 0, lo, hi)
    send = jnp.where(bit == 0, hi, lo)
    return keep, send


def butterfly_rs(x, axis, dim):
    n = lax.axis_size(axis)
    idx = lax.axis_index(axis)
    d = 1
    while d < n:
        bit = (idx // d) % 2
        keep, send = halves(x, dim, bit)
        pairs = [(i, i ^ d) for i in range(n)]
        x = keep + lax.ppermute(send, axis, pairs)
        d *= 2
    return x


def butterfly_ag(x, axis, dim):
    n = lax.axis_size(axis)
    idx = lax.axis_index(axis)
    d = n // 2
    while d >= 1:
        bit = (idx // d) % 2
        pairs = [(i, i ^ d) for i in range(n)]
        got = lax.ppermute(x, axis, pairs)
        first = jnp.where(bit == 0, x, got)
        second = jnp.where(bit == 0, got, x)
        x = jnp.concatenate([first, second], axis=dim)
        d //= 2
    return x


def pairs_of(n, stride, s):
    m = n // stride
    return [(i, ((i // stride + s) % m) * stride + i % stride) for i in range(n)]


def direct_rs(x, axis, stride=1):
    n = lax.axis_size(axis)
    m = n // stride
    g = lax.axis_index(axis) // stride
    xr = jnp.roll(x, -g, axis=0)
    total = xr[0]
    for s in range(1, m):
        total = total + lax.ppermute(xr[s], axis, pairs_of(n, stride, s))
    return total


def direct_ag(x, axis, stride=1):
    n = lax.axis_size(axis)
    m = n // stride
    g = lax.axis_index(axis) // stride
    got = [x] + [lax.ppermute(x, axis, pairs_of(n, stride, s)) for s in range(1, m)]
    rev = jnp.stack([got[(m - t) % m] for t in range(m)])
    return jnp.roll(rev, g, axis=0)


def pair_rs(x, axis):
    n = lax.axis_size(axis)
    bit = lax.axis_index(axis) % 2
    x = x.reshape((n // 2, 2) + x.shape[1:])
    keep = jnp.where(bit == 0, x[:, 0], x[:, 1])
    send = jnp.where(bit == 0, x[:, 1], x[:, 0])
    x = keep + lax.ppermute(send, axis, [(i, i ^ 1) for i in range(n)])
    return direct_rs(x, axis, 2)


def pair_ag(x, axis):
    n = lax.axis_size(axis)
    bit = lax.axis_index(axis) % 2
    x = direct_ag(x, axis, 2)
    got = lax.ppermute(x, axis, [(i, i ^ 1) for i in range(n)])
    first = jnp.where(bit == 0, x, got)
    second = jnp.where(bit == 0, got, x)
    return jnp.stack([first, second], axis=1).reshape((n,) + x.shape[1:])


def butterfly_all_reduce(x, axis, dim):
    n = lax.axis_size(axis)
    idx = lax.axis_index(axis)
    d = 1
    while d < n // 2:
        bit = (idx // d) % 2
        keep, send = halves(x, dim, bit)
        x = keep + lax.ppermute(send, axis, [(i, i ^ d) for i in range(n)])
        d *= 2
    x = x + lax.ppermute(x, axis, [(i, i ^ d) for i in range(n)])
    d //= 2
    while d >= 1:
        bit = (idx // d) % 2
        got = lax.ppermute(x, axis, [(i, i ^ d) for i in range(n)])
        first = jnp.where(bit == 0, x, got)
        second = jnp.where(bit == 0, got, x)
        x = jnp.concatenate([first, second], axis=dim)
        d //= 2
    return x


def z_then_pair(x, axis):
    n = lax.axis_size(axis)
    m = n // 2
    x = x.reshape((2, m) + x.shape[1:])
    x = jnp.moveaxis(x, 0, 1)
    x = direct_rs(x, axis, 2)
    x = x + lax.ppermute(x, axis, [(i, i ^ 1) for i in range(n)])
    x = direct_ag(x, axis, 2)
    return jnp.moveaxis(x, 1, 0).reshape((n,) + x.shape[2:])


def local(signal, w_init, h_init):
    steps_per = WIN // HOP
    frames_dev = signal.shape[0] // HOP
    tail = shifted(signal[: (steps_per - 1) * HOP], "tm", -1)
    lanes = HOP // 128
    tail = tail.reshape((steps_per - 1) * lanes, 128)
    local_bins = K // lax.axis_size("freq")
    win4 = hann_window().reshape(steps_per, HOP)
    tables = small_tables(lax.axis_index("freq") * local_bins, local_bins)
    power = power_kernel(signal.reshape(frames_dev * lanes, 128), tail, win4, tables, local_bins)
    factor_w = w_init
    factor_h = h_init
    rank = factor_w.shape[1]
    for step in range(ITERS):
        model = jnp.dot(factor_w, factor_h, precision=HI, preferred_element_type=jnp.float32)
        ratio = power / model
        numer = jnp.einsum("kr,kf->rf", factor_w, ratio, precision=HI)
        column_sums = jnp.sum(factor_w, axis=0)
        side = jnp.zeros((8, numer.shape[1]), jnp.float32).at[0, :rank].set(column_sums)
        both = butterfly_all_reduce(jnp.concatenate([numer, side]), "freq", 1)
        factor_h = factor_h * both[:rank] / both[rank, :rank][:, None]
        model = jnp.dot(factor_w, factor_h, precision=HI, preferred_element_type=jnp.float32)
        ratio = power / model
        row_sums = jnp.sum(factor_h, axis=1)
        spectral = jnp.einsum("kf,rf->kr", ratio, factor_h, precision=HI)
        n_tm = lax.axis_size("tm")
        chunks = spectral.reshape(n_tm, spectral.shape[0] // n_tm, rank)
        side = jnp.zeros((n_tm, 8, rank), jnp.float32).at[0, 0].set(row_sums)
        both = z_then_pair(jnp.concatenate([chunks, side], axis=1), "tm")
        spectral = both[:, :-8].reshape(spectral.shape)
        factor_w = factor_w * spectral / both[0, -8][None, :]
    return (factor_w, factor_h)


def solution(mesh):
    in_specs = (P("tm"), P("freq", None), P(None, "tm"))
    out_specs = (P("freq", None), P(None, "tm"))
    return jax.shard_map(local, mesh=mesh, in_specs=in_specs, out_specs=out_specs, check_vma=False)
```
